32 devices in a mesh: row: 4 (over y, x), col: 8 (over z, core).
Axes of the slice: x: 2, y: 2, z: 4, core: 2. Of those that a mesh axis runs over, the one named last changes fastest.
Arguments:
- left_blocks: bfloat16 [96, 32, 128, 128], P('col', 'row'), may hold values from -0.5 to 0.5
- left_cols: int32 [96, 32], P('col', 'row'), may hold values from 0 to 511, as said below
- right_blocks: bfloat16 [512, 4, 128, 128], P('col', 'row'), may hold values from -6 to 6
- right_cols: int32 [512, 4], P('col', 'row'), may hold values from 0 to 127, as said below
- keep_cols: int32 [96, 16], P('col', 'row'), may hold values from 0 to 127, as said below
Outputs:
- product_blocks: bfloat16 [96, 16, 128, 128], P('col', 'row')
The draws below stay inside these ranges and needn't reach their ends.
Inputs may be any that keep to these rules, and one draw needn't show every extreme that they name: `left_cols`: slot s of every block row names a block column in [(s // 4) * 64, (s // 4 + 1) * 64); the 4 slots of one range name distinct block columns. `right_cols`: entry [K, n] names a block column in [n * 32, (n + 1) * 32). `keep_cols`: slot k of every block row names a block column in [(k // 4) * 32, (k // 4 + 1) * 32); the 4 slots of one range name distinct block columns.
All inputs are finite; a program needn't handle non-finite values.
Results may differ from the reference program's by a relative error of at most 0.001.
Values may be sent and summed in bfloat16 or wider, within the bound.
No kernel may reach another device: no remote copies, remote signals or barrier semaphores. Data moves between devices by JAX's collectives and lax.ppermute only.
A program may use at most 192 MiB of HBM per device.

```python
import jax
import jax.numpy as jnp
from jax import lax

BS = 128
NB = 512
SA = 32
NJR = 32
KR = 4
MB = 96
NJ = 128
KC = 64
SAG = 4
N_ROW = 4


def common_pick(key):
    groups = NB // KC
    scores = jax.random.randint(jax.random.fold_in(key, 41), (groups, KC), 0, 1 << 20)
    scores = scores * KC + jnp.arange(KC, dtype=jnp.int32)[None, :]
    scores = scores.at[0, 0].set(1 << 30)
    picked = jnp.argsort(scores, axis=1, stable=True)[:, :SAG].astype(jnp.int32)
    marks = jnp.any(picked[:, :, None] == jnp.arange(KC, dtype=jnp.int32)[None, None, :], axis=1)
    return (picked, marks.reshape(NB))


def common_left(key):
    groups = NB // KC
    picked, marks = common_pick(key)
    scores = jax.random.randint(jax.random.fold_in(key, 11), (MB, groups, KC), 0, 1 << 20)
    scores = scores * KC + jnp.arange(KC, dtype=jnp.int32)[None, None, :]
    scores = scores.at[0, 0, 0].set(-2)
    scores = scores.at[0, groups - 1, KC - 1].set(-1)
    order = jnp.argsort(scores, axis=2, stable=True)[:, :, :SAG].astype(jnp.int32)
    special = jnp.arange(MB, dtype=jnp.int32) % 4 == 3
    order = jnp.where(special[:, None, None], picked[None, :, :], order)
    base = (jnp.arange(groups, dtype=jnp.int32) * KC)[None, :, None]
    return (order + base).reshape(MB, SA)


def common_right(key):
    ranges = NJ // NJR
    picked, marks = common_pick(key)
    offsets = jax.random.randint(jax.random.fold_in(key, 23), (NB, ranges), 0, NJR)
    shifts = jax.random.randint(jax.random.fold_in(key, 53), (ranges,), 0, NJR)
    near = jax.random.randint(jax.random.fold_in(key, 59), (NB, ranges), 0, KR)
    gathered = (shifts[None, :] + near) % NJR
    offsets = jnp.where(marks[:, None], gathered, offsets)
    offsets = offsets.at[0, 0].set(0)
    offsets = offsets.at[0, ranges - 1].set(NJR - 1)
    return offsets + (jnp.arange(ranges, dtype=jnp.int32) * NJR)[None, :]


def draw_left_cols(key, part):
    return common_left(key)


def draw_right_cols(key, part):
    return common_right(key)


def draw_keep_cols(key, part):
    ranges = NJ // NJR
    left = common_left(key)
    right = common_right(key)
    targets = jnp.take(right, left, axis=0)
    local = targets - (jnp.arange(ranges, dtype=jnp.int32) * NJR)[None, None, :]
    hits = jnp.sum((local[:, :, :, None] == jnp.arange(NJR, dtype=jnp.int32)[None, None, None, :]).astype(jnp.int32), axis=1)
    noise = jax.random.randint(jax.random.fold_in(key, 37), (MB, ranges, NJR), 0, 1 << 18)
    scores = (hits > 0).astype(jnp.int32) * (1 << 28) + noise * NJR + jnp.arange(NJR, dtype=jnp.int32)[None, None, :]
    scores = scores.at[0, 0, 0].set(1 << 30)
    scores = scores.at[0, ranges - 1, NJR - 1].set(1 << 30)
    order = jnp.argsort(-scores, axis=2, stable=True)[:, :, :KR].astype(jnp.int32)
    base = (jnp.arange(ranges, dtype=jnp.int32) * NJR)[None, :, None]
    return (order + base).reshape(MB, KR * ranges)


def shard_levels(rng, shape, pieces, smallest, largest):
    level = 1.0
    for position, parts in pieces:
        steps = jax.random.uniform(jax.random.fold_in(jax.random.fold_in(rng, 6), position), (parts,), jnp.float32, smallest / len(pieces), largest / len(pieces))
        level = level * jnp.repeat(jnp.exp(steps), shape[position] // parts).reshape((-1,) + (1,) * (len(shape) - 1 - position))
    return level


def centred(rng, dims, scale, limit, shards=(), held_as=jnp.bfloat16):
    drawn = scale * jax.random.normal(rng, dims, jnp.float32)
    if shards:
        drawn = drawn * shard_levels(rng, dims, shards, -0.22, 0.18)
    return jnp.clip(drawn, -limit, limit).astype(held_as)


def setup_inputs(seed: int = 0) -> dict:
    key_list = jax.random.split(jax.random.key(seed), 6)
    return {
        "left_blocks": centred(key_list[0], (MB, SA, BS, BS), BS ** -0.5, 0.5, ((0, 8), (1, 4))),
        "left_cols": draw_left_cols(jax.random.fold_in(key_list[5], 71), 0),
        "right_blocks": centred(key_list[2], (NB, N_ROW, BS, BS), 1.0, 6.0, ((0, 8), (1, 4))),
        "right_cols": draw_right_cols(jax.random.fold_in(key_list[5], 71), 0),
        "keep_cols": draw_keep_cols(jax.random.fold_in(key_list[5], 71), 0),
    }


def reference(left_blocks, left_cols, right_blocks, right_cols, keep_cols):
    def one_row(items):
        row_blocks, row_cols, row_keep = items
        chosen = jnp.take(right_blocks, row_cols, axis=0)
        targets = jnp.take(right_cols, row_cols, axis=0)
        terms = jnp.einsum("sxy,snyz->snxz", row_blocks.astype(jnp.float32), chosen.astype(jnp.float32), precision=lax.Precision.HIGHEST)
        summed = jnp.zeros((NJ, BS, BS), jnp.float32).at[targets.reshape(-1)].add(terms.reshape(-1, BS, BS))
        return jnp.take(summed, row_keep, axis=0).astype(jnp.bfloat16)

    return lax.map(one_row, (left_blocks, left_cols, keep_cols))
```

```python
import jax
import jax.numpy as jnp
from jax import lax
from jax.experimental import pallas as pl
from jax.experimental.pallas import tpu as pltpu
from jax.sharding import PartitionSpec as P

NJR = 32


def kept_slot(targets, kept):
    match = targets[:, :, None] == kept[:, None, :]
    found = jnp.any(match, axis=2)
    position = jnp.sum(
        match.astype(jnp.int32) * jnp.arange(kept.shape[1], dtype=jnp.int32)[None, None, :], axis=2
    )
    return jnp.where(found, position, kept.shape[1])


def product_kernel(kidx_ref, slot_ref, left_ref, right_hbm, out_ref, rbuf, sem, acc):
    i = pl.program_id(0)
    rows = pl.num_programs(0)
    slots = left_ref.shape[0]
    kr = out_ref.shape[0]

    def fetch(row, buf):
        for s in range(slots):
            pltpu.make_async_copy(
                right_hbm.at[kidx_ref[row * slots + s]], rbuf.at[buf, s], sem.at[buf, s]
            ).start()

    @pl.when(i == 0)
    def _():
        fetch(0, 0)

    buf = i % 2

    @pl.when(i + 1 < rows)
    def _():
        fetch(i + 1, 1 - buf)

    acc[...] = jnp.zeros_like(acc)
    for s in range(slots):
        pltpu.make_async_copy(right_hbm.at[0], rbuf.at[buf, s], sem.at[buf, s]).wait()
        term = jnp.dot(left_ref[s], rbuf[buf, s], preferred_element_type=jnp.float32)
        k = slot_ref[i * slots + s]
        acc[k] += term
    out_ref[...] = acc[0:kr].astype(out_ref.dtype)


def block_product(kidx, slot, panel_blocks, right_flat, kr):
    rows, slots, bs, _ = panel_blocks.shape
    grid_spec = pltpu.PrefetchScalarGridSpec(
        num_scalar_prefetch=2,
        grid=(rows,),
        in_specs=[
            pl.BlockSpec((None, slots, bs, bs), lambda i, kidx, slot: (i, 0, 0, 0)),
            pl.BlockSpec(memory_space=pl.ANY),
        ],
        out_specs=pl.BlockSpec((None, kr, bs, bs), lambda i, kidx, slot: (i, 0, 0, 0)),
        scratch_shapes=[
            pltpu.VMEM((2, slots, bs, bs), right_flat.dtype),
            pltpu.SemaphoreType.DMA((2, slots)),
            pltpu.VMEM((kr + 1, bs, bs), jnp.float32),
        ],
    )
    flops = 2 * rows * slots * bs * bs * bs
    nbytes = 2 * (2 * rows * slots * bs * bs + rows * kr * bs * bs)
    return pl.pallas_call(
        product_kernel,
        grid_spec=grid_spec,
        out_shape=jax.ShapeDtypeStruct((rows, kr, bs, bs), jnp.bfloat16),
        compiler_params=pltpu.CompilerParams(dimension_semantics=("arbitrary",)),
        cost_estimate=pl.CostEstimate(flops=flops, transcendentals=0, bytes_accessed=nbytes),
    )(kidx, slot, panel_blocks, right_flat)


def local(left_blocks, left_cols, right_blocks, right_cols, keep_cols):
    row_rank = lax.axis_index("row")
    kept = keep_cols - row_rank * NJR
    panel_blocks = lax.all_gather(left_blocks, "row", axis=1, tiled=True)
    panel_cols = lax.all_gather(left_cols, "row", axis=1, tiled=True)
    piece_blocks = lax.all_gather(right_blocks, "col", axis=0, tiled=True)
    piece_cols = lax.all_gather(right_cols, "col", axis=0, tiled=True)
    targets = jnp.take(piece_cols[:, 0], panel_cols, axis=0) - row_rank * NJR
    slot = kept_slot(targets, kept)
    right_flat = piece_blocks[:, 0]
    return block_product(
        panel_cols.reshape(-1), slot.reshape(-1), panel_blocks, right_flat, keep_cols.shape[1]
    )


def solution(mesh):
    in_specs = (
        P("col", "row", None, None),
        P("col", "row"),
        P("col", "row", None, None),
        P("col", "row"),
        P("col", "row"),
    )
    out_specs = P("col", "row", None, None)
    return jax.shard_map(local, mesh=mesh, in_specs=in_specs, out_specs=out_specs, check_vma=False)
```

```python
import jax
import jax.numpy as jnp
from jax import lax
from jax.experimental import pallas as pl
from jax.experimental.pallas import tpu as pltpu
from jax.sharding import PartitionSpec as P

NJR = 32


def kept_slot(targets, kept):
    match = targets[:, :, None] == kept[:, None, :]
    found = jnp.any(match, axis=2)
    position = jnp.sum(
        match.astype(jnp.int32) * jnp.arange(kept.shape[1], dtype=jnp.int32)[None, None, :], axis=2
    )
    return jnp.where(found, position, kept.shape[1])


def product_kernel(table_ref, *refs):
    n_pieces = len(refs) - 6
    pieces = refs[:n_pieces]
    right_hbm = refs[n_pieces]
    out_ref, lbuf, rbuf, sem, acc_ref = refs[n_pieces + 1:]
    i = pl.program_id(0)
    rows = pl.num_programs(0)
    per_piece = pieces[0].shape[1]
    slots = n_pieces * per_piece
    kr = out_ref.shape[0]

    def fetch(row, buf):
        for s in range(slots):
            at = row * slots + s
            pos = table_ref[1, at]
            pltpu.make_async_copy(
                pieces[s // per_piece].at[row, s % per_piece], lbuf.at[buf, pos], sem.at[0, buf, s]
            ).start()
            pltpu.make_async_copy(
                right_hbm.at[table_ref[0, at]], rbuf.at[buf, pos], sem.at[1, buf, s]
            ).start()

    @pl.when(i == 0)
    def _():
        fetch(0, 0)

    buf = i % 2

    @pl.when(i + 1 < rows)
    def _():
        fetch(i + 1, 1 - buf)

    for s in range(slots):
        pltpu.make_async_copy(pieces[0].at[0, 0], lbuf.at[buf, s], sem.at[0, buf, s]).wait()
        pltpu.make_async_copy(right_hbm.at[0], rbuf.at[buf, s], sem.at[1, buf, s]).wait()

    acc_ref[...] = jnp.zeros_like(acc_ref)
    acc = None
    for j in range(slots):
        at = i * slots + j
        term = jnp.dot(lbuf[buf, j], rbuf[buf, j], preferred_element_type=jnp.float32)
        acc = term if j == 0 else jnp.where(table_ref[3, at] != 0, term, acc + term)
        acc_ref[table_ref[2, at]] = acc
    out_ref[...] = acc_ref[0:kr].astype(out_ref.dtype)


def block_product(table, pieces, right_flat, kr):
    rows, per_piece, bs, _ = pieces[0].shape
    slots = per_piece * len(pieces)
    grid_spec = pltpu.PrefetchScalarGridSpec(
        num_scalar_prefetch=1,
        grid=(rows,),
        in_specs=[pl.BlockSpec(memory_space=pl.ANY)] * (len(pieces) + 1),
        out_specs=pl.BlockSpec((None, kr, bs, bs), lambda i, table: (i, 0, 0, 0)),
        scratch_shapes=[
            pltpu.VMEM((2, slots, bs, bs), pieces[0].dtype),
            pltpu.VMEM((2, slots, bs, bs), right_flat.dtype),
            pltpu.SemaphoreType.DMA((2, 2, slots)),
            pltpu.VMEM((kr + 1, bs, bs), jnp.float32),
        ],
    )
    flops = 2 * rows * slots * bs * bs * bs
    nbytes = 2 * (2 * rows * slots * bs * bs + rows * kr * bs * bs)
    return pl.pallas_call(
        product_kernel,
        grid_spec=grid_spec,
        out_shape=jax.ShapeDtypeStruct((rows, kr, bs, bs), jnp.bfloat16),
        compiler_params=pltpu.CompilerParams(dimension_semantics=("arbitrary",)),
        cost_estimate=pl.CostEstimate(flops=flops, transcendentals=0, bytes_accessed=nbytes),
    )(table, *pieces, right_flat)


def exchange(x, axis, n):
    out = [x]
    for d in range(1, n):
        perm = [(j, j ^ d) for j in range(n)]
        out.append(lax.ppermute(x, axis, perm))
    return out


def local(left_blocks, left_cols, right_blocks, right_cols, keep_cols):
    n_row = lax.psum(1, "row")
    row_rank = lax.axis_index("row")
    kept = keep_cols - row_rank * NJR
    pieces = exchange(left_blocks, "row", n_row)
    panel_cols = jnp.concatenate(exchange(left_cols, "row", n_row), axis=1)
    piece_blocks = lax.all_gather(right_blocks, "col", axis=0, tiled=True)
    piece_cols = lax.all_gather(right_cols, "col", axis=0, tiled=True)
    targets = jnp.take(piece_cols[:, 0], panel_cols, axis=0) - row_rank * NJR
    slot = kept_slot(targets, kept)
    rows, slots = slot.shape
    order = jnp.argsort(slot, axis=1, stable=True).astype(jnp.int32)
    position = jnp.argsort(order, axis=1).astype(jnp.int32)
    sorted_slot = jnp.take_along_axis(slot, order, axis=1)
    start = jnp.concatenate(
        [jnp.ones((rows, 1), jnp.int32), (sorted_slot[:, 1:] != sorted_slot[:, :-1]).astype(jnp.int32)],
        axis=1,
    )
    table = jnp.stack([panel_cols, position, sorted_slot, start]).reshape(4, rows * slots)
    return block_product(table, pieces, piece_blocks[:, 0], keep_cols.shape[1])


def solution(mesh):
    in_specs = (
        P("col", "row", None, None),
        P("col", "row"),
        P("col", "row", None, None),
        P("col", "row"),
        P("col", "row"),
    )
    out_specs = P("col", "row", None, None)
    return jax.shard_map(local, mesh=mesh, in_specs=in_specs, out_specs=out_specs, check_vma=False)
```

```python
import jax
import jax.numpy as jnp
from jax import lax
from jax.experimental import pallas as pl
from jax.experimental.pallas import tpu as pltpu
from jax.sharding import PartitionSpec as P

NJR = 32


def kept_slot(targets, kept):
    match = targets[:, :, None] == kept[:, None, :]
    found = jnp.any(match, axis=2)
    position = jnp.sum(
        match.astype(jnp.int32) * jnp.arange(kept.shape[1], dtype=jnp.int32)[None, None, :], axis=2
    )
    return jnp.where(found, position, kept.shape[1])


def product_kernel(table_ref, left_ref, right_hbm, out_ref, rbuf, sem, acc_ref):
    i = pl.program_id(0)
    rows = pl.num_programs(0)
    slots = left_ref.shape[0]
    kr = out_ref.shape[0]

    def fetch(row, buf):
        for s in range(slots):
            at = row * slots + s
            pltpu.make_async_copy(
                right_hbm.at[table_ref[0, at]], rbuf.at[buf, table_ref[1, at]], sem.at[buf, s]
            ).start()

    @pl.when(i == 0)
    def _():
        fetch(0, 0)

    buf = i % 2

    @pl.when(i + 1 < rows)
    def _():
        fetch(i + 1, 1 - buf)

    for s in range(slots):
        pltpu.make_async_copy(right_hbm.at[0], rbuf.at[buf, s], sem.at[buf, s]).wait()

    acc_ref[...] = jnp.zeros_like(acc_ref)
    acc = None
    for j in range(slots):
        at = i * slots + j
        term = jnp.dot(left_ref[table_ref[2, at]], rbuf[buf, j], preferred_element_type=jnp.float32)
        acc = term if j == 0 else jnp.where(table_ref[4, at] != 0, term, acc + term)
        acc_ref[table_ref[3, at]] = acc
    out_ref[...] = acc_ref[0:kr].astype(out_ref.dtype)


def block_product(table, panel, right_flat, kr):
    rows, slots, bs, _ = panel.shape
    grid_spec = pltpu.PrefetchScalarGridSpec(
        num_scalar_prefetch=1,
        grid=(rows,),
        in_specs=[
            pl.BlockSpec((None, slots, bs, bs), lambda i, table: (i, 0, 0, 0)),
            pl.BlockSpec(memory_space=pl.ANY),
        ],
        out_specs=pl.BlockSpec((None, kr, bs, bs), lambda i, table: (i, 0, 0, 0)),
        scratch_shapes=[
            pltpu.VMEM((2, slots, bs, bs), right_flat.dtype),
            pltpu.SemaphoreType.DMA((2, slots)),
            pltpu.VMEM((kr + 1, bs, bs), jnp.float32),
        ],
    )
    flops = 2 * rows * slots * bs * bs * bs
    nbytes = 2 * (2 * rows * slots * bs * bs + rows * kr * bs * bs)
    return pl.pallas_call(
        product_kernel,
        grid_spec=grid_spec,
        out_shape=jax.ShapeDtypeStruct((rows, kr, bs, bs), jnp.bfloat16),
        compiler_params=pltpu.CompilerParams(dimension_semantics=("arbitrary",)),
        cost_estimate=pl.CostEstimate(flops=flops, transcendentals=0, bytes_accessed=nbytes),
    )(table, panel, right_flat)


def exchange(x, axis, n):
    out = [x]
    for d in range(1, n):
        perm = [(j, j ^ d) for j in range(n)]
        out.append(lax.ppermute(x, axis, perm))
    return out


def local(left_blocks, left_cols, right_blocks, right_cols, keep_cols):
    n_row = lax.psum(1, "row")
    row_rank = lax.axis_index("row")
    kept = keep_cols - row_rank * NJR
    piece_blocks = lax.all_gather(right_blocks, "col", axis=0, tiled=True)
    panel_cols = jnp.concatenate(exchange(left_cols, "row", n_row), axis=1)
    left_blocks, panel_cols = lax.optimization_barrier((left_blocks, panel_cols))
    panel = jnp.concatenate(exchange(left_blocks, "row", n_row), axis=1)
    piece_cols = lax.all_gather(right_cols, "col", axis=0, tiled=True)
    targets = jnp.take(piece_cols[:, 0], panel_cols, axis=0) - row_rank * NJR
    slot = kept_slot(targets, kept)
    rows, slots = slot.shape
    order = jnp.argsort(slot, axis=1, stable=True).astype(jnp.int32)
    position = jnp.argsort(order, axis=1).astype(jnp.int32)
    sorted_slot = jnp.take_along_axis(slot, order, axis=1)
    start = jnp.concatenate(
        [jnp.ones((rows, 1), jnp.int32), (sorted_slot[:, 1:] != sorted_slot[:, :-1]).astype(jnp.int32)],
        axis=1,
    )
    table = jnp.stack([panel_cols, position, order, sorted_slot, start]).reshape(5, rows * slots)
    return block_product(table, panel, piece_blocks[:, 0], keep_cols.shape[1])


def solution(mesh):
    in_specs = (
        P("col", "row", None, None),
        P("col", "row"),
        P("col", "row", None, None),
        P("col", "row"),
        P("col", "row"),
    )
    out_specs = P("col", "row", None, None)
    return jax.shard_map(local, mesh=mesh, in_specs=in_specs, out_specs=out_specs, check_vma=False)
```

```python
import jax
import jax.numpy as jnp
from jax import lax
from jax.experimental import pallas as pl
from jax.experimental.pallas import tpu as pltpu
from jax.sharding import PartitionSpec as P

NJR = 32


def kept_slot(targets, kept):
    match = targets[:, :, None] == kept[:, None, :]
    found = jnp.any(match, axis=2)
    position = jnp.sum(
        match.astype(jnp.int32) * jnp.arange(kept.shape[1], dtype=jnp.int32)[None, None, :], axis=2
    )
    return jnp.where(found, position, kept.shape[1])


def product_kernel(table_ref, *refs):
    n_pieces = len(refs) - 7
    pieces = refs[:n_pieces]
    right_hbm, out_ref, rall, lbuf, rsem, lsem, acc_ref = refs[n_pieces:]
    i = pl.program_id(0)
    rows = pl.num_programs(0)
    per_piece = pieces[0].shape[1]
    slots = n_pieces * per_piece
    kr = out_ref.shape[0]
    n_chunks = rsem.shape[0]
    chunk = rall.shape[0] // n_chunks

    def right_copy(c):
        return pltpu.make_async_copy(
            right_hbm.at[pl.ds(c * chunk, chunk)], rall.at[pl.ds(c * chunk, chunk)], rsem.at[c]
        )

    def left_copy(row, buf, p):
        return pltpu.make_async_copy(
            pieces[p].at[row], lbuf.at[buf, pl.ds(p * per_piece, per_piece)], lsem.at[buf, p]
        )

    buf = i % 2

    @pl.when(i == 0)
    def _():
        for p in range(n_pieces):
            left_copy(0, 0, p).start()
        for c in range(n_chunks):
            right_copy(c).start()
        for c in range(n_chunks):
            right_copy(c).wait()

    @pl.when(i + 1 < rows)
    def _():
        for p in range(n_pieces):
            left_copy(i + 1, 1 - buf, p).start()

    for p in range(n_pieces):
        left_copy(0, buf, p).wait()

    acc_ref[...] = jnp.zeros_like(acc_ref)
    acc = None
    for j in range(slots):
        at = i * slots + j
        term = jnp.dot(
            lbuf[buf, table_ref[0, at]], rall[table_ref[1, at]], preferred_element_type=jnp.float32
        )
        acc = term if j == 0 else jnp.where(table_ref[3, at] != 0, term, acc + term)
        acc_ref[table_ref[2, at]] = acc
    out_ref[...] = acc_ref[0:kr].astype(out_ref.dtype)


def block_product(table, pieces, right_flat, kr):
    rows, per_piece, bs, _ = pieces[0].shape
    slots = per_piece * len(pieces)
    n_right = right_flat.shape[0]
    n_chunks = 8 if n_right % 8 == 0 else 1
    grid_spec = pltpu.PrefetchScalarGridSpec(
        num_scalar_prefetch=1,
        grid=(rows,),
        in_specs=[pl.BlockSpec(memory_space=pl.ANY)] * (len(pieces) + 1),
        out_specs=pl.BlockSpec((None, kr, bs, bs), lambda i, table: (i, 0, 0, 0)),
        scratch_shapes=[
            pltpu.VMEM((n_right, bs, bs), right_flat.dtype),
            pltpu.VMEM((2, slots, bs, bs), pieces[0].dtype),
            pltpu.SemaphoreType.DMA((n_chunks,)),
            pltpu.SemaphoreType.DMA((2, len(pieces))),
            pltpu.VMEM((kr + 1, bs, bs), jnp.float32),
        ],
    )
    flops = 2 * rows * slots * bs * bs * bs
    nbytes = 2 * (n_right * bs * bs + rows * slots * bs * bs + rows * kr * bs * bs)
    return pl.pallas_call(
        product_kernel,
        grid_spec=grid_spec,
        out_shape=jax.ShapeDtypeStruct((rows, kr, bs, bs), jnp.bfloat16),
        compiler_params=pltpu.CompilerParams(
            dimension_semantics=("arbitrary",), vmem_limit_bytes=48 * 1024 * 1024
        ),
        cost_estimate=pl.CostEstimate(flops=flops, transcendentals=0, bytes_accessed=nbytes),
    )(table, *pieces, right_flat)


def exchange(x, axis, n):
    out = [x]
    for d in range(1, n):
        perm = [(j, j ^ d) for j in range(n)]
        out.append(lax.ppermute(x, axis, perm))
    return out


def local(left_blocks, left_cols, right_blocks, right_cols, keep_cols):
    n_row = lax.psum(1, "row")
    row_rank = lax.axis_index("row")
    kept = keep_cols - row_rank * NJR
    piece_blocks = lax.all_gather(right_blocks, "col", axis=0, tiled=True)
    panel_cols = jnp.concatenate(exchange(left_cols, "row", n_row), axis=1)
    left_blocks, panel_cols = lax.optimization_barrier((left_blocks, panel_cols))
    pieces = exchange(left_blocks, "row", n_row)
    piece_cols = lax.all_gather(right_cols, "col", axis=0, tiled=True)
    targets = jnp.take(piece_cols[:, 0], panel_cols, axis=0) - row_rank * NJR
    slot = kept_slot(targets, kept)
    rows, slots = slot.shape
    order = jnp.argsort(slot, axis=1, stable=True).astype(jnp.int32)
    sorted_slot = jnp.take_along_axis(slot, order, axis=1)
    start = jnp.concatenate(
        [jnp.ones((rows, 1), jnp.int32), (sorted_slot[:, 1:] != sorted_slot[:, :-1]).astype(jnp.int32)],
        axis=1,
    )
    sorted_cols = jnp.take_along_axis(panel_cols, order, axis=1)
    table = jnp.stack([order, sorted_cols, sorted_slot, start]).reshape(4, rows * slots)
    return block_product(table, pieces, piece_blocks[:, 0], keep_cols.shape[1])


def solution(mesh):
    in_specs = (
        P("col", "row", None, None),
        P("col", "row"),
        P("col", "row", None, None),
        P("col", "row"),
        P("col", "row"),
    )
    out_specs = P("col", "row", None, None)
    return jax.shard_map(local, mesh=mesh, in_specs=in_specs, out_specs=out_specs, check_vma=False)
```

```python
import jax
import jax.numpy as jnp
from jax import lax
from jax.experimental import pallas as pl
from jax.experimental.pallas import tpu as pltpu
from jax.sharding import PartitionSpec as P

NJR = 32


def kept_slot(targets, kept):
    match = targets[:, :, None] == kept[:, None, :]
    found = jnp.any(match, axis=2)
    position = jnp.sum(
        match.astype(jnp.int32) * jnp.arange(kept.shape[1], dtype=jnp.int32)[None, None, :], axis=2
    )
    return jnp.where(found, position, kept.shape[1])


def product_kernel(table_ref, *refs):
    n_pieces = len(refs) - 6
    pieces = refs[:n_pieces]
    right_hbm, out_ref, lbuf, rbuf, sem, acc_ref = refs[n_pieces:]
    i = pl.program_id(0)
    rows = pl.num_programs(0)
    per_piece = pieces[0].shape[1]
    slots = n_pieces * per_piece
    kr = out_ref.shape[0]

    def left_copy(row, buf, s, pos):
        return pltpu.make_async_copy(
            pieces[s // per_piece].at[row, s % per_piece], lbuf.at[buf, pos], sem.at[0, buf, s]
        )

    def right_copy(k, buf, s, pos):
        return pltpu.make_async_copy(right_hbm.at[k], rbuf.at[buf, pos], sem.at[1, buf, s])

    def fetch(row, buf):
        for s in range(slots):
            at = row * slots + s

            @pl.when(table_ref[2, at] != 0)
            def _():
                pos = table_ref[1, at]
                left_copy(row, buf, s, pos).start()
                right_copy(table_ref[0, at], buf, s, pos).start()

    @pl.when(i == 0)
    def _():
        fetch(0, 0)

    buf = i % 2

    @pl.when(i + 1 < rows)
    def _():
        fetch(i + 1, 1 - buf)

    for s in range(slots):
        at = i * slots + s

        @pl.when(table_ref[2, at] != 0)
        def _():
            left_copy(0, buf, s, s).wait()
            right_copy(0, buf, s, s).wait()

    acc_ref[...] = jnp.zeros_like(acc_ref)
    acc = None
    for j in range(slots):
        at = i * slots + j
        term = jnp.dot(lbuf[buf, j], rbuf[buf, j], preferred_element_type=jnp.float32)
        acc = term if j == 0 else jnp.where(table_ref[4, at] != 0, term, acc + term)
        acc_ref[table_ref[3, at]] = acc
    out_ref[...] = acc_ref[0:kr].astype(out_ref.dtype)


def block_product(table, pieces, right_flat, kr):
    rows, per_piece, bs, _ = pieces[0].shape
    slots = per_piece * len(pieces)
    grid_spec = pltpu.PrefetchScalarGridSpec(
        num_scalar_prefetch=1,
        grid=(rows,),
        in_specs=[pl.BlockSpec(memory_space=pl.ANY)] * (len(pieces) + 1),
        out_specs=pl.BlockSpec((None, kr, bs, bs), lambda i, table: (i, 0, 0, 0)),
        scratch_shapes=[
            pltpu.VMEM((2, slots, bs, bs), pieces[0].dtype),
            pltpu.VMEM((2, slots, bs, bs), right_flat.dtype),
            pltpu.SemaphoreType.DMA((2, 2, slots)),
            pltpu.VMEM((kr + 1, bs, bs), jnp.float32),
        ],
    )
    flops = 2 * rows * slots * bs * bs * bs
    nbytes = 2 * (2 * rows * slots * bs * bs + rows * kr * bs * bs)
    return pl.pallas_call(
        product_kernel,
        grid_spec=grid_spec,
        out_shape=jax.ShapeDtypeStruct((rows, kr, bs, bs), jnp.bfloat16),
        compiler_params=pltpu.CompilerParams(dimension_semantics=("arbitrary",)),
        cost_estimate=pl.CostEstimate(flops=flops, transcendentals=0, bytes_accessed=nbytes),
    )(table, *pieces, right_flat)


def exchange(x, axis, n):
    out = [x]
    for d in range(1, n):
        perm = [(j, j ^ d) for j in range(n)]
        out.append(lax.ppermute(x, axis, perm))
    return out


def local(left_blocks, left_cols, right_blocks, right_cols, keep_cols):
    n_row = lax.psum(1, "row")
    row_rank = lax.axis_index("row")
    kept = keep_cols - row_rank * NJR
    piece_blocks = lax.all_gather(right_blocks, "col", axis=0, tiled=True)
    panel_cols = jnp.concatenate(exchange(left_cols, "row", n_row), axis=1)
    left_blocks, panel_cols = lax.optimization_barrier((left_blocks, panel_cols))
    pieces = exchange(left_blocks, "row", n_row)
    piece_cols = lax.all_gather(right_cols, "col", axis=0, tiled=True)
    targets = jnp.take(piece_cols[:, 0], panel_cols, axis=0) - row_rank * NJR
    slot = kept_slot(targets, kept)
    rows, slots = slot.shape
    order = jnp.argsort(slot, axis=1, stable=True).astype(jnp.int32)
    sorted_slot = jnp.take_along_axis(slot, order, axis=1)
    start = jnp.concatenate(
        [jnp.ones((rows, 1), jnp.int32), (sorted_slot[:, 1:] != sorted_slot[:, :-1]).astype(jnp.int32)],
        axis=1,
    )
    position = jnp.argsort(order, axis=1).astype(jnp.int32)
    used = (slot < keep_cols.shape[1]).astype(jnp.int32)
    table = jnp.stack([panel_cols, position, used, sorted_slot, start]).reshape(5, rows * slots)
    return block_product(table, pieces, piece_blocks[:, 0], keep_cols.shape[1])


def solution(mesh):
    in_specs = (
        P("col", "row", None, None),
        P("col", "row"),
        P("col", "row", None, None),
        P("col", "row"),
        P("col", "row"),
    )
    out_specs = P("col", "row", None, None)
    return jax.shard_map(local, mesh=mesh, in_specs=in_specs, out_specs=out_specs, check_vma=False)
```

```python
import jax
import jax.numpy as jnp
from jax import lax
from jax.experimental import pallas as pl
from jax.experimental.pallas import tpu as pltpu
from jax.sharding import PartitionSpec as P

NJR = 32
CHUNK = 4


def kept_slot(targets, kept):
    match = targets[:, :, None] == kept[:, None, :]
    found = jnp.any(match, axis=2)
    position = jnp.sum(
        match.astype(jnp.int32) * jnp.arange(kept.shape[1], dtype=jnp.int32)[None, None, :], axis=2
    )
    return jnp.where(found, position, kept.shape[1])


def product_kernel(table_ref, *refs):
    n_pieces = len(refs) - 7
    pieces = refs[:n_pieces]
    right_hbm, out_ref, lbuf, rbuf, sem, acc_ref, carry_ref = refs[n_pieces:]
    i = pl.program_id(0)
    rows = pl.num_programs(0)
    per_piece = pieces[0].shape[1]
    slots = n_pieces * per_piece
    kr = out_ref.shape[0]

    def left_copy(row, buf, s, pos):
        return pltpu.make_async_copy(
            pieces[s // per_piece].at[row, s % per_piece], lbuf.at[buf, pos], sem.at[0, buf, s]
        )

    def right_copy(k, buf, s, pos):
        return pltpu.make_async_copy(right_hbm.at[k], rbuf.at[buf, pos], sem.at[1, buf, s])

    def fetch(row, buf):
        for s in range(slots):
            at = row * slots + s

            @pl.when(table_ref[2, at] != 0)
            def _():
                pos = table_ref[1, at]
                left_copy(row, buf, s, pos).start()
                right_copy(table_ref[0, at], buf, s, pos).start()

    @pl.when(i == 0)
    def _():
        fetch(0, 0)

    buf = i % 2

    @pl.when(i + 1 < rows)
    def _():
        fetch(i + 1, 1 - buf)

    for s in range(slots):
        at = i * slots + s

        @pl.when(table_ref[2, at] != 0)
        def _():
            left_copy(0, buf, s, s).wait()
            right_copy(0, buf, s, s).wait()

    acc_ref[...] = jnp.zeros_like(acc_ref)
    n_used = table_ref[5, i * slots]
    for c in range(0, slots, CHUNK):

        @pl.when(c < n_used)
        def _():
            acc = None if c == 0 else carry_ref[...]
            for j in range(c, min(c + CHUNK, slots)):
                at = i * slots + j
                term = jnp.dot(lbuf[buf, j], rbuf[buf, j], preferred_element_type=jnp.float32)
                acc = term if j == 0 else jnp.where(table_ref[4, at] != 0, term, acc + term)
                acc_ref[table_ref[3, at]] = acc
            carry_ref[...] = acc

    out_ref[...] = acc_ref[0:kr].astype(out_ref.dtype)


def block_product(table, pieces, right_flat, kr):
    rows, per_piece, bs, _ = pieces[0].shape
    slots = per_piece * len(pieces)
    grid_spec = pltpu.PrefetchScalarGridSpec(
        num_scalar_prefetch=1,
        grid=(rows,),
        in_specs=[pl.BlockSpec(memory_space=pl.ANY)] * (len(pieces) + 1),
        out_specs=pl.BlockSpec((None, kr, bs, bs), lambda i, table: (i, 0, 0, 0)),
        scratch_shapes=[
            pltpu.VMEM((2, slots, bs, bs), pieces[0].dtype),
            pltpu.VMEM((2, slots, bs, bs), right_flat.dtype),
            pltpu.SemaphoreType.DMA((2, 2, slots)),
            pltpu.VMEM((kr + 1, bs, bs), jnp.float32),
            pltpu.VMEM((bs, bs), jnp.float32),
        ],
    )
    flops = 2 * rows * slots * bs * bs * bs
    nbytes = 2 * (2 * rows * slots * bs * bs + rows * kr * bs * bs)
    return pl.pallas_call(
        product_kernel,
        grid_spec=grid_spec,
        out_shape=jax.ShapeDtypeStruct((rows, kr, bs, bs), jnp.bfloat16),
        compiler_params=pltpu.CompilerParams(dimension_semantics=("arbitrary",)),
        cost_estimate=pl.CostEstimate(flops=flops, transcendentals=0, bytes_accessed=nbytes),
    )(table, *pieces, right_flat)


def exchange(x, axis, n):
    out = [x]
    for d in range(1, n):
        perm = [(j, j ^ d) for j in range(n)]
        out.append(lax.ppermute(x, axis, perm))
    return out


def local(left_blocks, left_cols, right_blocks, right_cols, keep_cols):
    n_row = lax.psum(1, "row")
    row_rank = lax.axis_index("row")
    kept = keep_cols - row_rank * NJR
    piece_blocks = lax.all_gather(right_blocks, "col", axis=0, tiled=True)
    panel_cols = jnp.concatenate(exchange(left_cols, "row", n_row), axis=1)
    left_blocks, panel_cols = lax.optimization_barrier((left_blocks, panel_cols))
    pieces = exchange(left_blocks, "row", n_row)
    piece_cols = lax.all_gather(right_cols, "col", axis=0, tiled=True)
    targets = jnp.take(piece_cols[:, 0], panel_cols, axis=0) - row_rank * NJR
    slot = kept_slot(targets, kept)
    rows, slots = slot.shape
    order = jnp.argsort(slot, axis=1, stable=True).astype(jnp.int32)
    sorted_slot = jnp.take_along_axis(slot, order, axis=1)
    start = jnp.concatenate(
        [jnp.ones((rows, 1), jnp.int32), (sorted_slot[:, 1:] != sorted_slot[:, :-1]).astype(jnp.int32)],
        axis=1,
    )
    position = jnp.argsort(order, axis=1).astype(jnp.int32)
    used = (slot < keep_cols.shape[1]).astype(jnp.int32)
    n_used = jnp.broadcast_to(jnp.sum(used, axis=1, keepdims=True), (rows, slots))
    table = jnp.stack([panel_cols, position, used, sorted_slot, start, n_used]).reshape(6, rows * slots)
    return block_product(table, pieces, piece_blocks[:, 0], keep_cols.shape[1])


def solution(mesh):
    in_specs = (
        P("col", "row", None, None),
        P("col", "row"),
        P("col", "row", None, None),
        P("col", "row"),
        P("col", "row"),
    )
    out_specs = P("col", "row", None, None)
    return jax.shard_map(local, mesh=mesh, in_specs=in_specs, out_specs=out_specs, check_vma=False)
```

```python
import jax
import jax.numpy as jnp
from jax import lax
from jax.experimental import pallas as pl
from jax.experimental.pallas import tpu as pltpu
from jax.sharding import PartitionSpec as P

NJR = 32


def kept_slot(targets, kept):
    match = targets[:, :, None] == kept[:, None, :]
    found = jnp.any(match, axis=2)
    position = jnp.sum(
        match.astype(jnp.int32) * jnp.arange(kept.shape[1], dtype=jnp.int32)[None, None, :], axis=2
    )
    return jnp.where(found, position, kept.shape[1])


def product_kernel(table_ref, *refs):
    n_pieces = len(refs) - 6
    pieces = refs[:n_pieces]
    right_hbm, out_ref, lbuf, rbuf, sem, acc_ref = refs[n_pieces:]
    i = pl.program_id(0)
    steps = pl.num_programs(0)
    per_piece = pieces[0].shape[1]
    slots = n_pieces * per_piece
    per_step, kr = out_ref.shape[0], out_ref.shape[1]

    def left_copy(row, buf, r, s, pos):
        return pltpu.make_async_copy(
            pieces[s // per_piece].at[row, s % per_piece], lbuf.at[buf, r, pos], sem.at[0, buf, r, s]
        )

    def right_copy(k, buf, r, s, pos):
        return pltpu.make_async_copy(right_hbm.at[k], rbuf.at[buf, r, pos], sem.at[1, buf, r, s])

    def fetch(step, buf):
        for r in range(per_step):
            row = step * per_step + r
            for s in range(slots):
                at = row * slots + s

                @pl.when(table_ref[2, at] != 0)
                def _():
                    pos = table_ref[1, at]
                    left_copy(row, buf, r, s, pos).start()
                    right_copy(table_ref[0, at], buf, r, s, pos).start()

    @pl.when(i == 0)
    def _():
        fetch(0, 0)

    buf = i % 2

    @pl.when(i + 1 < steps)
    def _():
        fetch(i + 1, 1 - buf)

    for r in range(per_step):
        row = i * per_step + r
        for s in range(slots):
            at = row * slots + s

            @pl.when(table_ref[2, at] != 0)
            def _():
                left_copy(0, buf, r, s, s).wait()
                right_copy(0, buf, r, s, s).wait()

    for r in range(per_step):
        row = i * per_step + r
        acc_ref[...] = jnp.zeros_like(acc_ref)
        acc = None
        for j in range(slots):
            at = row * slots + j
            term = jnp.dot(lbuf[buf, r, j], rbuf[buf, r, j], preferred_element_type=jnp.float32)
            acc = term if j == 0 else jnp.where(table_ref[4, at] != 0, term, acc + term)
            acc_ref[table_ref[3, at]] = acc
        out_ref[r] = acc_ref[0:kr].astype(out_ref.dtype)


def block_product(table, pieces, right_flat, kr):
    rows, per_piece, bs, _ = pieces[0].shape
    slots = per_piece * len(pieces)
    per_step = 2 if rows % 2 == 0 else 1
    grid_spec = pltpu.PrefetchScalarGridSpec(
        num_scalar_prefetch=1,
        grid=(rows // per_step,),
        in_specs=[pl.BlockSpec(memory_space=pl.ANY)] * (len(pieces) + 1),
        out_specs=pl.BlockSpec((per_step, kr, bs, bs), lambda i, table: (i, 0, 0, 0)),
        scratch_shapes=[
            pltpu.VMEM((2, per_step, slots, bs, bs), pieces[0].dtype),
            pltpu.VMEM((2, per_step, slots, bs, bs), right_flat.dtype),
            pltpu.SemaphoreType.DMA((2, 2, per_step, slots)),
            pltpu.VMEM((kr + 1, bs, bs), jnp.float32),
        ],
    )
    flops = 2 * rows * slots * bs * bs * bs
    nbytes = 2 * (2 * rows * slots * bs * bs + rows * kr * bs * bs)
    return pl.pallas_call(
        product_kernel,
        grid_spec=grid_spec,
        out_shape=jax.ShapeDtypeStruct((rows, kr, bs, bs), jnp.bfloat16),
        compiler_params=pltpu.CompilerParams(dimension_semantics=("arbitrary",)),
        cost_estimate=pl.CostEstimate(flops=flops, transcendentals=0, bytes_accessed=nbytes),
    )(table, *pieces, right_flat)


def exchange(x, axis, n):
    out = [x]
    for d in range(1, n):
        perm = [(j, j ^ d) for j in range(n)]
        out.append(lax.ppermute(x, axis, perm))
    return out


def local(left_blocks, left_cols, right_blocks, right_cols, keep_cols):
    n_row = lax.psum(1, "row")
    row_rank = lax.axis_index("row")
    kept = keep_cols - row_rank * NJR
    piece_blocks = lax.all_gather(right_blocks, "col", axis=0, tiled=True)
    panel_cols = jnp.concatenate(exchange(left_cols, "row", n_row), axis=1)
    left_blocks, panel_cols = lax.optimization_barrier((left_blocks, panel_cols))
    pieces = exchange(left_blocks, "row", n_row)
    piece_cols = lax.all_gather(right_cols, "col", axis=0, tiled=True)
    targets = jnp.take(piece_cols[:, 0], panel_cols, axis=0) - row_rank * NJR
    slot = kept_slot(targets, kept)
    rows, slots = slot.shape
    order = jnp.argsort(slot, axis=1, stable=True).astype(jnp.int32)
    sorted_slot = jnp.take_along_axis(slot, order, axis=1)
    start = jnp.concatenate(
        [jnp.ones((rows, 1), jnp.int32), (sorted_slot[:, 1:] != sorted_slot[:, :-1]).astype(jnp.int32)],
        axis=1,
    )
    position = jnp.argsort(order, axis=1).astype(jnp.int32)
    used = (slot < keep_cols.shape[1]).astype(jnp.int32)
    table = jnp.stack([panel_cols, position, used, sorted_slot, start]).reshape(5, rows * slots)
    return block_product(table, pieces, piece_blocks[:, 0], keep_cols.shape[1])


def solution(mesh):
    in_specs = (
        P("col", "row", None, None),
        P("col", "row"),
        P("col", "row", None, None),
        P("col", "row"),
        P("col", "row"),
    )
    out_specs = P("col", "row", None, None)
    return jax.shard_map(local, mesh=mesh, in_specs=in_specs, out_specs=out_specs, check_vma=False)
```

```python
import jax
import jax.numpy as jnp
from jax import lax
from jax.experimental import pallas as pl
from jax.experimental.pallas import tpu as pltpu
from jax.sharding import PartitionSpec as P

NJR = 32


def kept_slot(targets, kept):
    match = targets[:, :, None] == kept[:, None, :]
    found = jnp.any(match, axis=2)
    position = jnp.sum(
        match.astype(jnp.int32) * jnp.arange(kept.shape[1], dtype=jnp.int32)[None, None, :], axis=2
    )
    return jnp.where(found, position, kept.shape[1])


def product_kernel(table_ref, *refs):
    n_pieces = len(refs) - 6
    pieces = refs[:n_pieces]
    right_hbm, out_ref, lbuf, rbuf, sem, acc_ref = refs[n_pieces:]
    i = pl.program_id(0)
    steps = pl.num_programs(0)
    per_piece = pieces[0].shape[1]
    slots = n_pieces * per_piece
    per_step, kr = out_ref.shape[0], out_ref.shape[1]

    def left_copy(row, buf, r, p):
        return pltpu.make_async_copy(
            pieces[p].at[row], lbuf.at[buf, r, pl.ds(p * per_piece, per_piece)], sem.at[0, buf, r, p]
        )

    def right_copy(k, buf, r, s, pos):
        return pltpu.make_async_copy(right_hbm.at[k], rbuf.at[buf, r, pos], sem.at[1, buf, r, s])

    def fetch(step, buf):
        for r in range(per_step):
            row = step * per_step + r
            for p in range(n_pieces):
                left_copy(row, buf, r, p).start()
            for s in range(slots):
                at = row * slots + s

                @pl.when(table_ref[2, at] != 0)
                def _():
                    right_copy(table_ref[0, at], buf, r, s, table_ref[1, at]).start()

    @pl.when(i == 0)
    def _():
        fetch(0, 0)

    buf = i % 2

    @pl.when(i + 1 < steps)
    def _():
        fetch(i + 1, 1 - buf)

    for r in range(per_step):
        row = i * per_step + r
        for p in range(n_pieces):
            left_copy(0, buf, r, p).wait()
        for s in range(slots):
            at = row * slots + s

            @pl.when(table_ref[2, at] != 0)
            def _():
                right_copy(0, buf, r, s, s).wait()

    for r in range(per_step):
        row = i * per_step + r
        acc_ref[...] = jnp.zeros_like(acc_ref)
        acc = None
        for j in range(slots):
            at = row * slots + j
            term = jnp.dot(
                lbuf[buf, r, table_ref[5, at]], rbuf[buf, r, j], preferred_element_type=jnp.float32
            )
            acc = term if j == 0 else jnp.where(table_ref[4, at] != 0, term, acc + term)
            acc_ref[table_ref[3, at]] = acc
        out_ref[r] = acc_ref[0:kr].astype(out_ref.dtype)


def block_product(table, pieces, right_flat, kr):
    rows, per_piece, bs, _ = pieces[0].shape
    slots = per_piece * len(pieces)
    per_step = 2 if rows % 2 == 0 else 1
    grid_spec = pltpu.PrefetchScalarGridSpec(
        num_scalar_prefetch=1,
        grid=(rows // per_step,),
        in_specs=[pl.BlockSpec(memory_space=pl.ANY)] * (len(pieces) + 1),
        out_specs=pl.BlockSpec((per_step, kr, bs, bs), lambda i, table: (i, 0, 0, 0)),
        scratch_shapes=[
            pltpu.VMEM((2, per_step, slots, bs, bs), pieces[0].dtype),
            pltpu.VMEM((2, per_step, slots, bs, bs), right_flat.dtype),
            pltpu.SemaphoreType.DMA((2, 2, per_step, slots)),
            pltpu.VMEM((kr + 1, bs, bs), jnp.float32),
        ],
    )
    flops = 2 * rows * slots * bs * bs * bs
    nbytes = 2 * (2 * rows * slots * bs * bs + rows * kr * bs * bs)
    return pl.pallas_call(
        product_kernel,
        grid_spec=grid_spec,
        out_shape=jax.ShapeDtypeStruct((rows, kr, bs, bs), jnp.bfloat16),
        compiler_params=pltpu.CompilerParams(dimension_semantics=("arbitrary",)),
        cost_estimate=pl.CostEstimate(flops=flops, transcendentals=0, bytes_accessed=nbytes),
    )(table, *pieces, right_flat)


def exchange(x, axis, n):
    out = [x]
    for d in range(1, n):
        perm = [(j, j ^ d) for j in range(n)]
        out.append(lax.ppermute(x, axis, perm))
    return out


def local(left_blocks, left_cols, right_blocks, right_cols, keep_cols):
    n_row = lax.psum(1, "row")
    row_rank = lax.axis_index("row")
    kept = keep_cols - row_rank * NJR
    piece_blocks = lax.all_gather(right_blocks, "col", axis=0, tiled=True)
    panel_cols = jnp.concatenate(exchange(left_cols, "row", n_row), axis=1)
    left_blocks, panel_cols = lax.optimization_barrier((left_blocks, panel_cols))
    pieces = exchange(left_blocks, "row", n_row)
    piece_cols = lax.all_gather(right_cols, "col", axis=0, tiled=True)
    targets = jnp.take(piece_cols[:, 0], panel_cols, axis=0) - row_rank * NJR
    slot = kept_slot(targets, kept)
    rows, slots = slot.shape
    order = jnp.argsort(slot, axis=1, stable=True).astype(jnp.int32)
    sorted_slot = jnp.take_along_axis(slot, order, axis=1)
    start = jnp.concatenate(
        [jnp.ones((rows, 1), jnp.int32), (sorted_slot[:, 1:] != sorted_slot[:, :-1]).astype(jnp.int32)],
        axis=1,
    )
    position = jnp.argsort(order, axis=1).astype(jnp.int32)
    used = (slot < keep_cols.shape[1]).astype(jnp.int32)
    table = jnp.stack([panel_cols, position, used, sorted_slot, start, order]).reshape(6, rows * slots)
    return block_product(table, pieces, piece_blocks[:, 0], keep_cols.shape[1])


def solution(mesh):
    in_specs = (
        P("col", "row", None, None),
        P("col", "row"),
        P("col", "row", None, None),
        P("col", "row"),
        P("col", "row"),
    )
    out_specs = P("col", "row", None, None)
    return jax.shard_map(local, mesh=mesh, in_specs=in_specs, out_specs=out_specs, check_vma=False)
```

```python
import jax
import jax.numpy as jnp
from jax import lax
from jax.experimental import pallas as pl
from jax.experimental.pallas import tpu as pltpu
from jax.sharding import PartitionSpec as P

NJR = 32


def kept_slot(targets, kept):
    match = targets[:, :, None] == kept[:, None, :]
    found = jnp.any(match, axis=2)
    position = jnp.sum(
        match.astype(jnp.int32) * jnp.arange(kept.shape[1], dtype=jnp.int32)[None, None, :], axis=2
    )
    return jnp.where(found, position, kept.shape[1])


def product_kernel(table_ref, *refs):
    n_pieces = len(refs) - 6
    pieces = refs[:n_pieces]
    right_hbm, out_ref, lbuf, rbuf, sem, acc_ref = refs[n_pieces:]
    i = pl.program_id(0)
    steps = pl.num_programs(0)
    per_piece = pieces[0].shape[1]
    slots = n_pieces * per_piece
    per_step, kr = out_ref.shape[0], out_ref.shape[1]

    def left_copy(row, buf, r, s, pos):
        return pltpu.make_async_copy(
            pieces[s // per_piece].at[row, s % per_piece], lbuf.at[buf, r, pos], sem.at[0, buf, r, s]
        )

    def right_copy(k, buf, r, s, pos):
        return pltpu.make_async_copy(right_hbm.at[k], rbuf.at[buf, r, pos], sem.at[1, buf, r, s])

    def fetch(step, buf):
        for r in range(per_step):
            row = step * per_step + r
            for s in range(slots):
                at = row * slots + s

                @pl.when(table_ref[2, at] != 0)
                def _():
                    pos = table_ref[1, at]
                    left_copy(row, buf, r, s, pos).start()
                    right_copy(table_ref[0, at], buf, r, s, pos).start()

    @pl.when(i == 0)
    def _():
        fetch(0, 0)

    buf = i % 2

    @pl.when(i + 1 < steps)
    def _():
        fetch(i + 1, 1 - buf)

    for r in range(per_step):
        row = i * per_step + r
        for s in range(slots):
            at = row * slots + s

            @pl.when(table_ref[2, at] != 0)
            def _():
                left_copy(0, buf, r, s, s).wait()
                right_copy(0, buf, r, s, s).wait()

    for r in range(per_step):
        row = i * per_step + r
        acc_ref[...] = jnp.zeros_like(acc_ref)
        acc = None
        for j in range(slots):
            at = row * slots + j
            term = jnp.dot(lbuf[buf, r, j], rbuf[buf, r, j], preferred_element_type=jnp.float32)
            acc = term if j == 0 else jnp.where(table_ref[4, at] != 0, term, acc + term)
            acc_ref[table_ref[3, at]] = acc
        out_ref[r] = acc_ref[0:kr].astype(out_ref.dtype)


def block_product(table, pieces, right_flat, kr):
    rows, per_piece, bs, _ = pieces[0].shape
    slots = per_piece * len(pieces)
    per_step = 3 if rows % 3 == 0 else 1
    grid_spec = pltpu.PrefetchScalarGridSpec(
        num_scalar_prefetch=1,
        grid=(rows // per_step,),
        in_specs=[pl.BlockSpec(memory_space=pl.ANY)] * (len(pieces) + 1),
        out_specs=pl.BlockSpec((per_step, kr, bs, bs), lambda i, table: (i, 0, 0, 0)),
        scratch_shapes=[
            pltpu.VMEM((2, per_step, slots, bs, bs), pieces[0].dtype),
            pltpu.VMEM((2, per_step, slots, bs, bs), right_flat.dtype),
            pltpu.SemaphoreType.DMA((2, 2, per_step, slots)),
            pltpu.VMEM((kr + 1, bs, bs), jnp.float32),
        ],
    )
    flops = 2 * rows * slots * bs * bs * bs
    nbytes = 2 * (2 * rows * slots * bs * bs + rows * kr * bs * bs)
    return pl.pallas_call(
        product_kernel,
        grid_spec=grid_spec,
        out_shape=jax.ShapeDtypeStruct((rows, kr, bs, bs), jnp.bfloat16),
        compiler_params=pltpu.CompilerParams(dimension_semantics=("arbitrary",)),
        cost_estimate=pl.CostEstimate(flops=flops, transcendentals=0, bytes_accessed=nbytes),
    )(table, *pieces, right_flat)


def exchange(x, axis, n):
    out = [x]
    for d in range(1, n):
        perm = [(j, j ^ d) for j in range(n)]
        out.append(lax.ppermute(x, axis, perm))
    return out


def local(left_blocks, left_cols, right_blocks, right_cols, keep_cols):
    n_row = lax.psum(1, "row")
    row_rank = lax.axis_index("row")
    kept = keep_cols - row_rank * NJR
    piece_blocks = lax.all_gather(right_blocks, "col", axis=0, tiled=True)
    panel_cols = jnp.concatenate(exchange(left_cols, "row", n_row), axis=1)
    left_blocks, panel_cols = lax.optimization_barrier((left_blocks, panel_cols))
    pieces = exchange(left_blocks, "row", n_row)
    piece_cols = lax.all_gather(right_cols, "col", axis=0, tiled=True)
    targets = jnp.take(piece_cols[:, 0], panel_cols, axis=0) - row_rank * NJR
    slot = kept_slot(targets, kept)
    rows, slots = slot.shape
    order = jnp.argsort(slot, axis=1, stable=True).astype(jnp.int32)
    sorted_slot = jnp.take_along_axis(slot, order, axis=1)
    start = jnp.concatenate(
        [jnp.ones((rows, 1), jnp.int32), (sorted_slot[:, 1:] != sorted_slot[:, :-1]).astype(jnp.int32)],
        axis=1,
    )
    position = jnp.argsort(order, axis=1).astype(jnp.int32)
    used = (slot < keep_cols.shape[1]).astype(jnp.int32)
    table = jnp.stack([panel_cols, position, used, sorted_slot, start]).reshape(5, rows * slots)
    return block_product(table, pieces, piece_blocks[:, 0], keep_cols.shape[1])


def solution(mesh):
    in_specs = (
        P("col", "row", None, None),
        P("col", "row"),
        P("col", "row", None, None),
        P("col", "row"),
        P("col", "row"),
    )
    out_specs = P("col", "row", None, None)
    return jax.shard_map(local, mesh=mesh, in_specs=in_specs, out_specs=out_specs, check_vma=False)
```
